512 devices in a mesh: tm: 64 (over y, x, core), head: 8 (over z).
Axes of the slice: x: 4, y: 8, z: 8, core: 2. Of those that a mesh axis runs over, the one named last changes fastest.
Arguments:
- queries: bfloat16 [24576, 5120], P('tm', 'head')
- keys: bfloat16 [24576, 5120], P('tm', 'head')
- values: bfloat16 [24576, 5120], P('tm', 'head')
- text_keys: bfloat16 [512, 5120], P('tm', 'head'), may hold values from -6 to 6
- text_values: bfloat16 [512, 5120], P('tm', 'head')
- out_weight: bfloat16 [5120, 5120], P('head', 'tm'), may hold values from -0.25 to 0.25
- windows: int32 [64], replicated, may hold values from 0 to 4, as said below
- lengths: int32 [64], replicated, may hold values from 96 to 384, as said below
Outputs:
- mixed: bfloat16 [24576, 5120], P('tm', 'head')
The draws below stay inside these ranges and needn't reach their ends.
Inputs may be any that keep to these rules, and one draw needn't show every extreme that they name: windows reach 4 for some frame in every draw. `lengths`: some frame is full in every draw.
All inputs are finite; a program needn't handle non-finite values.
Results may differ from the reference program's by a relative error of at most 0.014.
Values may be sent and summed in bfloat16 or wider, within the bound.
No kernel may reach another device: no remote copies, remote signals or barrier semaphores. Data moves between devices by JAX's collectives and lax.ppermute only.
A program may use at most 64 MiB of HBM per device.

```python
import math
import jax
import jax.numpy as jnp
from jax import lax

HEADS = 40
HD = 128
TXT = 512
TPF = 384
WIN = 4
D = 5120
FRAMES = 64
N_HEAD = 8


def joint_fields(key):
    key_part = jax.random.fold_in(key, 11)
    query_part = jax.random.fold_in(key, 12)
    keys_f = jnp.clip(1.4 * jax.random.normal(key_part, (FRAMES, TPF, D), jnp.float32), -5.0, 5.0)
    query = jnp.clip(1.4 * jax.random.normal(query_part, (FRAMES, TPF, D), jnp.float32), -5.0, 5.0)
    return (query, keys_f)


def draw_queries(key, part):
    return joint_fields(key)[0].reshape(FRAMES * TPF, D).astype(jnp.bfloat16)


def draw_keys(key, part):
    return joint_fields(key)[1].reshape(FRAMES * TPF, D).astype(jnp.bfloat16)


def draw_values(key, part):
    means = jax.random.normal(jax.random.fold_in(key, 21), (FRAMES, 1, D), jnp.float32)
    rough = 0.5 * jax.random.normal(jax.random.fold_in(key, 22), (FRAMES, TPF, D), jnp.float32)
    return jnp.clip(means + rough, -5.0, 5.0).reshape(FRAMES * TPF, D).astype(jnp.bfloat16)


def draw_text_values(key, part):
    means = jax.random.normal(jax.random.fold_in(key, 31), (1, D), jnp.float32)
    rough = 0.5 * jax.random.normal(jax.random.fold_in(key, 32), (TXT, D), jnp.float32)
    return jnp.clip(means + rough, -5.0, 5.0).astype(jnp.bfloat16)


def draw_windows(key, part):
    drawn = jax.random.randint(jax.random.fold_in(key, 41), (FRAMES,), 0, WIN + 1)
    chosen = jax.random.randint(jax.random.fold_in(key, 42), (), 0, FRAMES)
    return drawn.at[chosen].set(WIN).astype(jnp.int32)


def draw_lengths(key, part):
    drawn = jax.random.randint(jax.random.fold_in(key, 51), (FRAMES,), TPF // 4, TPF + 1)
    chosen = jax.random.randint(jax.random.fold_in(key, 52), (), 0, FRAMES)
    return drawn.at[chosen].set(TPF).astype(jnp.int32)


def with_spikes(values, own_key, source, target, blocks, factor):
    owner, partner = [(jnp.arange(values.shape[position]) // (values.shape[position] // blocks)).reshape([-1 if axis == position else 1 for axis in range(values.ndim)]) for position in (source, target)]
    chosen = jax.random.permutation(own_key, blocks)[partner]
    strong = (owner == chosen) | (owner == (partner + blocks // 2) % blocks)
    return jnp.where(strong, factor * values, values)


def shard_levels(own_key, dims, cuts, low, top_value):
    factor_of, own = 1.0, jax.random.fold_in(own_key, 6)
    for dim, blocks in cuts:
        draws = jnp.exp(jax.random.uniform(jax.random.fold_in(own, dim), (blocks,), jnp.float32, low / len(cuts), top_value / len(cuts)))
        factor_of = factor_of * jnp.repeat(draws, dims[dim] // blocks).reshape([-1 if axis == dim else 1 for axis in range(len(dims))])
    return factor_of


def scatter_about(rng, shape, width, bound, pieces=(), kind=jnp.bfloat16):
    level = shard_levels(rng, shape, pieces, -0.22, 0.18) if pieces else 1.0
    values = jax.random.normal(rng, shape, jnp.float32) * width * level
    return jnp.minimum(jnp.maximum(values, -bound), bound).astype(kind)


def noise_with(key, extent, width, bound, cuts, heavy, held_as=jnp.bfloat16):
    result = width * jax.random.normal(key, extent, jnp.float32)
    if cuts:
        result = result * shard_levels(key, extent, cuts, -0.22, 0.18)
    return jnp.clip(with_spikes(result, jax.random.fold_in(key, 3), *heavy), -bound, bound).astype(held_as)


def setup_inputs(seed: int = 0) -> dict:
    seeds = jax.random.split(jax.random.key(seed), 9)
    return {
        "queries": draw_queries(jax.random.fold_in(seeds[8], 71), 0),
        "keys": draw_keys(jax.random.fold_in(seeds[8], 71), 0),
        "values": draw_values(jax.random.fold_in(seeds[8], 71), 0),
        "text_keys": scatter_about(seeds[3], (TXT, D), 1.4, 6.0, ((0, 64), (1, 8))),
        "text_values": draw_text_values(jax.random.fold_in(seeds[8], 71), 0),
        "out_weight": noise_with(seeds[5], (D, D), D ** -0.5, 0.25, ((0, 8), (1, 64)), (0, 1, 64, 4.0)),
        "windows": draw_windows(jax.random.fold_in(seeds[8], 71), 0),
        "lengths": draw_lengths(jax.random.fold_in(seeds[8], 71), 0),
    }


def reference(queries, keys, values, text_keys, text_values, out_weight, windows, lengths):
    scale = 1.0 / math.sqrt(HD)
    group = D // N_HEAD
    query_all = queries.reshape(FRAMES, TPF, HEADS, HD)
    blank = jnp.zeros((WIN, TPF, HEADS, HD), keys.dtype)
    keys_pad = jnp.concatenate([blank, keys.reshape(FRAMES, TPF, HEADS, HD)], axis=0)
    values_pad = jnp.concatenate([blank, values.reshape(FRAMES, TPF, HEADS, HD)], axis=0)
    text_k = text_keys.reshape(TXT, HEADS, HD).astype(jnp.float32)
    text_v = text_values.reshape(TXT, HEADS, HD).astype(jnp.float32)

    def one_frame(frame):
        frame = frame.astype(jnp.int32)
        window_k = lax.dynamic_slice_in_dim(keys_pad, frame, WIN + 1, 0)
        window_v = lax.dynamic_slice_in_dim(values_pad, frame, WIN + 1, 0)
        distance = WIN - jnp.arange(WIN + 1, dtype=jnp.int32)
        source = frame - distance
        source_len = lengths[jnp.maximum(source, 0)]
        usable = (distance <= windows[frame]) & (source >= 0)
        key_mask = usable[:, None] & (jnp.arange(TPF, dtype=jnp.int32)[None, :] < source_len[:, None])
        key_mask = jnp.concatenate([key_mask.reshape(-1), jnp.ones((TXT,), bool)])
        all_k = jnp.concatenate([window_k.reshape((WIN + 1) * TPF, HEADS, HD).astype(jnp.float32), text_k], axis=0)
        all_v = jnp.concatenate([window_v.reshape((WIN + 1) * TPF, HEADS, HD).astype(jnp.float32), text_v], axis=0)
        query_f = query_all[frame].astype(jnp.float32)
        scores = jnp.einsum('qhd,khd->hqk', query_f, all_k) * scale
        scores = jnp.where(key_mask[None, None, :], scores, -jnp.inf)
        top = lax.optimization_barrier(jnp.max(scores, axis=-1, keepdims=True))
        weights = jnp.exp(scores - top)
        total = lax.optimization_barrier(jnp.sum(weights, axis=-1))
        weights_b = weights.astype(jnp.bfloat16).astype(jnp.float32)
        attended = jnp.einsum('hqk,khd->qhd', weights_b, all_v) / jnp.transpose(total)[:, :, None]
        attended = attended.astype(jnp.bfloat16).reshape(TPF, D)
        summed = jnp.zeros((TPF, D), jnp.float32)
        for index in range(N_HEAD):
            piece = jnp.dot(attended[:, index * group:(index + 1) * group], out_weight[index * group:(index + 1) * group], preferred_element_type=jnp.float32)
            summed = summed + piece.astype(jnp.bfloat16).astype(jnp.float32)
        return summed.astype(jnp.bfloat16)
    mixed = lax.map(one_frame, jnp.arange(FRAMES, dtype=jnp.int32))
    return mixed.reshape(FRAMES * TPF, D)
```

```python
import math

import jax
import jax.numpy as jnp
from jax import lax
from jax.sharding import PartitionSpec as P

HD = 128
WIN = 4


def from_behind(value, axis, steps):
    count = lax.axis_size(axis)
    initial, last = (max(0, -steps), min(count, count - steps))
    return lax.ppermute(value, axis, [(source, source + steps) for source in range(initial, last)])


def gather_text(text_keys, text_values):
    width = text_keys.shape[1]
    both = jnp.concatenate([text_keys, text_values], axis=1)
    full = lax.all_gather(both, "tm", axis=0, tiled=True)
    return full[:, :width], full[:, width:]


def on_device(queries, keys, values, text_keys, text_values, out_weight, windows, lengths):
    rows = queries.shape[0]
    width = queries.shape[1]
    local_heads = width // HD
    groups = lax.axis_size("head")
    scale = 1.0 / math.sqrt(HD)
    position = lax.axis_index("tm")
    text_k, text_v = gather_text(text_keys, text_values)
    weight_all = lax.all_gather(out_weight, "tm", axis=1, tiled=True)
    kv = jnp.stack([keys, values])
    kv_list = [kv]
    for step in range(1, WIN + 1):
        kv_list.append(from_behind(kv, "tm", step))
    token_ids = jnp.arange(rows, dtype=jnp.int32)
    own_window = windows[position]
    mask_list = []
    for step in range(WIN + 1):
        source = position - step
        usable = (step <= own_window) & (source >= 0)
        source_len = lengths[jnp.maximum(source, 0)]
        mask_list.append(usable & (token_ids < source_len))
    mask_list.append(jnp.ones((text_k.shape[0],), bool))
    key_mask = jnp.concatenate(mask_list)
    all_keys = jnp.concatenate([p[0] for p in kv_list] + [text_k], axis=0)
    all_values = jnp.concatenate([p[1] for p in kv_list] + [text_v], axis=0)
    head_outputs = []
    for head_index in range(local_heads):
        lower = head_index * HD
        query_h = queries[:, lower : lower + HD]
        key_h = all_keys[:, lower : lower + HD]
        value_h = all_values[:, lower : lower + HD]
        scores = (
            lax.dot_general(
                query_h, key_h, (((1,), (1,)), ((), ())), preferred_element_type=jnp.float32
            )
            * scale
        )
        scores = jnp.where(key_mask[None, :], scores, -jnp.inf)
        top = jnp.max(scores, axis=-1, keepdims=True)
        weights = jnp.exp(scores - top)
        total = jnp.sum(weights, axis=-1, keepdims=True)
        attended = (
            jnp.dot(weights.astype(jnp.bfloat16), value_h, preferred_element_type=jnp.float32)
            / total
        )
        head_outputs.append(attended.astype(jnp.bfloat16))
    attended_all = jnp.concatenate(head_outputs, axis=1)
    w3 = weight_all.reshape(width, groups, weight_all.shape[1] // groups)
    partial_out = jnp.einsum("rk,kgc->grc", attended_all, w3, preferred_element_type=jnp.float32)
    mixed = lax.psum_scatter(partial_out.astype(jnp.bfloat16), "head", scatter_dimension=0, tiled=True)
    return mixed.reshape(rows, -1)


def solution(mesh):
    return jax.shard_map(
        on_device,
        mesh=mesh,
        in_specs=(
            P("tm", "head"),
            P("tm", "head"),
            P("tm", "head"),
            P("tm", "head"),
            P("tm", "head"),
            P("head", "tm"),
            P(),
            P(),
        ),
        out_specs=P("tm", "head"),
        check_vma=False,
    )
```

```python
import math

import jax
import jax.numpy as jnp
from jax import lax
from jax.sharding import PartitionSpec as P

HD = 128
WIN = 4


def from_behind(value, axis, steps):
    count = lax.axis_size(axis)
    initial, last = (max(0, -steps), min(count, count - steps))
    return lax.ppermute(value, axis, [(source, source + steps) for source in range(initial, last)])


FRAME_AXES = ("y", "x", "c")


def gather_frames(value, axis):
    for name in reversed(FRAME_AXES):
        value = lax.all_gather(value, name, axis=axis, tiled=True)
    return value


def gather_text(text_keys, text_values):
    width = text_keys.shape[1]
    both = jnp.concatenate([text_keys, text_values], axis=1)
    full = gather_frames(both, 0)
    return full[:, :width], full[:, width:]


def on_device(queries, keys, values, text_keys, text_values, out_weight, windows, lengths):
    rows = queries.shape[0]
    width = queries.shape[1]
    local_heads = width // HD
    groups = lax.axis_size("head")
    scale = 1.0 / math.sqrt(HD)
    position = lax.axis_index(FRAME_AXES)
    text_k, text_v = gather_text(text_keys, text_values)
    weight_all = gather_frames(out_weight, 1)
    kv = jnp.stack([keys, values])
    kv_list = [kv]
    for step in range(1, WIN + 1):
        kv_list.append(from_behind(kv, FRAME_AXES, step))
    token_ids = jnp.arange(rows, dtype=jnp.int32)
    own_window = windows[position]
    mask_list = []
    for step in range(WIN + 1):
        source = position - step
        usable = (step <= own_window) & (source >= 0)
        source_len = lengths[jnp.maximum(source, 0)]
        mask_list.append(usable & (token_ids < source_len))
    mask_list.append(jnp.ones((text_k.shape[0],), bool))
    key_mask = jnp.concatenate(mask_list)
    all_keys = jnp.concatenate([p[0] for p in kv_list] + [text_k], axis=0)
    all_values = jnp.concatenate([p[1] for p in kv_list] + [text_v], axis=0)
    head_outputs = []
    for head_index in range(local_heads):
        lower = head_index * HD
        query_h = queries[:, lower : lower + HD]
        key_h = all_keys[:, lower : lower + HD]
        value_h = all_values[:, lower : lower + HD]
        scores = (
            lax.dot_general(
                query_h, key_h, (((1,), (1,)), ((), ())), preferred_element_type=jnp.float32
            )
            * scale
        )
        scores = jnp.where(key_mask[None, :], scores, -jnp.inf)
        top = jnp.max(scores, axis=-1, keepdims=True)
        weights = jnp.exp(scores - top)
        total = jnp.sum(weights, axis=-1, keepdims=True)
        attended = (
            jnp.dot(weights.astype(jnp.bfloat16), value_h, preferred_element_type=jnp.float32)
            / total
        )
        head_outputs.append(attended.astype(jnp.bfloat16))
    attended_all = jnp.concatenate(head_outputs, axis=1)
    w3 = weight_all.reshape(width, groups, weight_all.shape[1] // groups)
    partial_out = jnp.einsum("rk,kgc->grc", attended_all, w3, preferred_element_type=jnp.float32)
    mixed = lax.psum_scatter(partial_out.astype(jnp.bfloat16), "head", scatter_dimension=0, tiled=True)
    return mixed.reshape(rows, -1)


def solution(mesh):
    frames = mesh.devices.shape[0]
    cores = 2
    xs = 4 if frames % (4 * cores) == 0 else 1
    grid = mesh.devices.reshape(frames // (xs * cores), xs, cores, mesh.devices.shape[1])
    fine = jax.sharding.Mesh(grid, FRAME_AXES + ("head",))
    return jax.shard_map(
        on_device,
        mesh=fine,
        in_specs=(
            P(FRAME_AXES, "head"),
            P(FRAME_AXES, "head"),
            P(FRAME_AXES, "head"),
            P(FRAME_AXES, "head"),
            P(FRAME_AXES, "head"),
            P("head", FRAME_AXES),
            P(),
            P(),
        ),
        out_specs=P(FRAME_AXES, "head"),
        check_vma=False,
    )
```

```python
import math

import jax
import jax.numpy as jnp
from jax import lax
from jax.sharding import PartitionSpec as P

HD = 128
WIN = 4
FRAME_AXES = ("y", "x", "c")
CHIP_AXES = ("y", "x")


def shift_frames(value, steps):
    count = lax.axis_size(FRAME_AXES)
    return lax.ppermute(value, FRAME_AXES, [(source, source + steps) for source in range(count - steps)])


def ring_gather(value, axis):
    count = lax.axis_size(axis)
    pieces = [value]
    for step in range(1, count):
        pieces.append(lax.ppermute(value, axis, [(source, (source + step) % count) for source in range(count)]))
    return jnp.concatenate(pieces, axis=0)


def swap_cores(value):
    return lax.ppermute(value, "c", [(0, 1), (1, 0)])


def on_device(queries, keys, values, text_keys, text_values, out_weight, windows, lengths):
    rows = queries.shape[0]
    width = queries.shape[1]
    local_heads = width // HD
    groups = lax.axis_size("head")
    scale = 1.0 / math.sqrt(HD)
    position = lax.axis_index(FRAME_AXES)
    core = lax.axis_index("c")
    first_core = core == 0

    text_both = jnp.concatenate([text_keys, text_values], axis=1)
    text_half = ring_gather(ring_gather(text_both, "x"), "y")
    text_all = jnp.concatenate([text_half, swap_cores(text_half)], axis=0)
    text_k, text_v = text_all[:, :width], text_all[:, width:]

    weight_half = lax.all_gather(out_weight, CHIP_AXES, axis=1, tiled=True)
    weight_pair = jnp.stack([weight_half, swap_cores(weight_half)])

    own = jnp.stack([keys, values])
    back2 = shift_frames(own, 2)
    back4 = shift_frames(own, 4)
    back1 = swap_cores(jnp.where(first_core, own, back2))
    back3 = swap_cores(jnp.where(first_core, back2, back4))
    kv_list = [own, back1, back2, back3, back4]

    token_ids = jnp.arange(rows, dtype=jnp.int32)
    own_window = windows[position]
    mask_list = []
    for step in range(WIN + 1):
        source = position - step
        usable = (step <= own_window) & (source >= 0)
        source_len = lengths[jnp.maximum(source, 0)]
        mask_list.append(usable & (token_ids < source_len))
    mask_list.append(jnp.ones((text_k.shape[0],), bool))
    key_mask = jnp.concatenate(mask_list)
    all_keys = jnp.concatenate([p[0] for p in kv_list] + [text_k], axis=0)
    all_values = jnp.concatenate([p[1] for p in kv_list] + [text_v], axis=0)
    head_outputs = []
    for head_index in range(local_heads):
        lower = head_index * HD
        query_h = queries[:, lower : lower + HD]
        key_h = all_keys[:, lower : lower + HD]
        value_h = all_values[:, lower : lower + HD]
        scores = (
            lax.dot_general(
                query_h, key_h, (((1,), (1,)), ((), ())), preferred_element_type=jnp.float32
            )
            * scale
        )
        scores = jnp.where(key_mask[None, :], scores, -jnp.inf)
        top = jnp.max(scores, axis=-1, keepdims=True)
        weights = jnp.exp(scores - top)
        total = jnp.sum(weights, axis=-1, keepdims=True)
        attended = (
            jnp.dot(weights.astype(jnp.bfloat16), value_h, preferred_element_type=jnp.float32)
            / total
        )
        head_outputs.append(attended.astype(jnp.bfloat16))
    attended_all = jnp.concatenate(head_outputs, axis=1)
    ys = lax.axis_size("y")
    xs = lax.axis_size("x")
    block = out_weight.shape[1]
    w5 = weight_pair.reshape(2, width, ys, xs, block)
    partial_out = jnp.einsum("rk,ckyxn->yrcxn", attended_all, w5, preferred_element_type=jnp.float32)
    partial_out = partial_out.reshape(groups, rows, -1)
    mixed = lax.psum_scatter(partial_out.astype(jnp.bfloat16), "head", scatter_dimension=0, tiled=True)
    mixed = mixed.reshape(rows, 2, xs, block)
    mixed = jnp.where(first_core, mixed, mixed[:, ::-1])
    return mixed.transpose(0, 2, 1, 3).reshape(rows, -1)


def solution(mesh):
    frames, heads = mesh.devices.shape
    cores = 2
    xs = 4 if frames % (4 * cores) == 0 else 1
    grid = mesh.devices.reshape(frames // (xs * cores), xs, cores, heads)
    fine = jax.sharding.Mesh(grid, FRAME_AXES + ("head",))
    return jax.shard_map(
        on_device,
        mesh=fine,
        in_specs=(
            P(FRAME_AXES, "head"),
            P(FRAME_AXES, "head"),
            P(FRAME_AXES, "head"),
            P(FRAME_AXES, "head"),
            P(FRAME_AXES, "head"),
            P("head", FRAME_AXES),
            P(),
            P(),
        ),
        out_specs=P(FRAME_AXES, "head"),
        check_vma=False,
    )
```

```python
import math

import jax
import jax.numpy as jnp
from jax import lax
from jax.sharding import PartitionSpec as P

HD = 128
WIN = 4
FRAME_AXES = ("y", "x", "c")
CHIP_AXES = ("y", "x")


def shift_frames(value, steps):
    count = lax.axis_size(FRAME_AXES)
    return lax.ppermute(value, FRAME_AXES, [(source, source + steps) for source in range(count - steps)])


def ring_gather(value, axis):
    count = lax.axis_size(axis)
    pieces = [value]
    for step in range(1, count):
        pieces.append(lax.ppermute(value, axis, [(source, (source + step) % count) for source in range(count)]))
    return jnp.concatenate(pieces, axis=0)


def swap_cores(value):
    return lax.ppermute(value, "c", [(0, 1), (1, 0)])


def on_device(queries, keys, values, text_keys, text_values, out_weight, windows, lengths):
    rows = queries.shape[0]
    width = queries.shape[1]
    local_heads = width // HD
    groups = lax.axis_size("head")
    scale = 1.0 / math.sqrt(HD)
    position = lax.axis_index(FRAME_AXES)
    core = lax.axis_index("c")
    first_core = core == 0

    text_both = jnp.concatenate([text_keys, text_values], axis=1)
    tokens = text_both.shape[0]
    chips = lax.axis_size(CHIP_AXES)
    block = out_weight.shape[1]
    text_cols = text_both.reshape(width, -1)
    packed = jnp.concatenate([out_weight, text_cols], axis=1)
    packed = lax.all_gather(packed, CHIP_AXES, axis=1, tiled=True).reshape(width, chips, -1)
    weight_half = packed[:, :, :block].reshape(width, chips * block)
    text_half = packed[:, :, block:].reshape(tokens, -1, chips, text_cols.shape[1])
    text_half = text_half.transpose(2, 0, 1, 3).reshape(chips * tokens, 2 * width)
    text_all = jnp.concatenate([text_half, swap_cores(text_half)], axis=0)
    text_k, text_v = text_all[:, :width], text_all[:, width:]
    weight_pair = jnp.stack([weight_half, swap_cores(weight_half)])

    own = jnp.stack([keys, values])
    back2 = shift_frames(own, 2)
    back4 = shift_frames(own, 4)
    back1 = swap_cores(jnp.where(first_core, own, back2))
    back3 = swap_cores(jnp.where(first_core, back2, back4))
    kv_list = [own, back1, back2, back3, back4]

    token_ids = jnp.arange(rows, dtype=jnp.int32)
    own_window = windows[position]
    mask_list = []
    for step in range(WIN + 1):
        source = position - step
        usable = (step <= own_window) & (source >= 0)
        source_len = lengths[jnp.maximum(source, 0)]
        mask_list.append(usable & (token_ids < source_len))
    mask_list.append(jnp.ones((text_k.shape[0],), bool))
    key_mask = jnp.concatenate(mask_list)
    all_keys = jnp.concatenate([p[0] for p in kv_list] + [text_k], axis=0)
    all_values = jnp.concatenate([p[1] for p in kv_list] + [text_v], axis=0)
    head_outputs = []
    for head_index in range(local_heads):
        lower = head_index * HD
        query_h = queries[:, lower : lower + HD]
        key_h = all_keys[:, lower : lower + HD]
        value_h = all_values[:, lower : lower + HD]
        scores = (
            lax.dot_general(
                query_h, key_h, (((1,), (1,)), ((), ())), preferred_element_type=jnp.float32
            )
            * scale
        )
        scores = jnp.where(key_mask[None, :], scores, -jnp.inf)
        top = jnp.max(scores, axis=-1, keepdims=True)
        weights = jnp.exp(scores - top)
        total = jnp.sum(weights, axis=-1, keepdims=True)
        attended = (
            jnp.dot(weights.astype(jnp.bfloat16), value_h, preferred_element_type=jnp.float32)
            / total
        )
        head_outputs.append(attended.astype(jnp.bfloat16))
    attended_all = jnp.concatenate(head_outputs, axis=1)
    ys = lax.axis_size("y")
    xs = lax.axis_size("x")
    w5 = weight_pair.reshape(2, width, ys, xs, block)
    partial_out = jnp.einsum("rk,ckyxn->yrcxn", attended_all, w5, preferred_element_type=jnp.float32)
    partial_out = partial_out.reshape(groups, rows, -1)
    mixed = lax.psum_scatter(partial_out.astype(jnp.bfloat16), "head", scatter_dimension=0, tiled=True)
    mixed = mixed.reshape(rows, 2, xs, block)
    mixed = jnp.where(first_core, mixed, mixed[:, ::-1])
    return mixed.transpose(0, 2, 1, 3).reshape(rows, -1)


def solution(mesh):
    frames, heads = mesh.devices.shape
    cores = 2
    xs = 4 if frames % (4 * cores) == 0 else 1
    grid = mesh.devices.reshape(frames // (xs * cores), xs, cores, heads)
    fine = jax.sharding.Mesh(grid, FRAME_AXES + ("head",))
    return jax.shard_map(
        on_device,
        mesh=fine,
        in_specs=(
            P(FRAME_AXES, "head"),
            P(FRAME_AXES, "head"),
            P(FRAME_AXES, "head"),
            P(FRAME_AXES, "head"),
            P(FRAME_AXES, "head"),
            P("head", FRAME_AXES),
            P(),
            P(),
        ),
        out_specs=P(FRAME_AXES, "head"),
        check_vma=False,
    )
```

```python
import math

import jax
import jax.numpy as jnp
from jax import lax
from jax.sharding import PartitionSpec as P

HD = 128
WIN = 4
FRAME_AXES = ("y", "x", "c")
CHIP_AXES = ("y", "x")


def shift_frames(value, steps):
    count = lax.axis_size(FRAME_AXES)
    return lax.ppermute(value, FRAME_AXES, [(source, source + steps) for source in range(count - steps)])


def ring_gather(value, axis):
    count = lax.axis_size(axis)
    pieces = [value]
    for step in range(1, count):
        pieces.append(lax.ppermute(value, axis, [(source, (source + step) % count) for source in range(count)]))
    return jnp.concatenate(pieces, axis=0)


def swap_cores(value):
    return lax.ppermute(value, "c", [(0, 1), (1, 0)])


def on_device(queries, keys, values, text_keys, text_values, out_weight, windows, lengths):
    rows = queries.shape[0]
    width = queries.shape[1]
    local_heads = width // HD
    groups = lax.axis_size("head")
    scale = 1.0 / math.sqrt(HD)
    position = lax.axis_index(FRAME_AXES)
    core = lax.axis_index("c")
    first_core = core == 0

    own = jnp.stack([keys, values])
    back2 = shift_frames(own, 2)
    back4 = shift_frames(own, 4)
    back1 = swap_cores(jnp.where(first_core, own, back2))
    back3 = swap_cores(jnp.where(first_core, back2, back4))
    kv_list = [own, back1, back2, back3, back4]

    token_ids = jnp.arange(rows, dtype=jnp.int32)
    own_window = windows[position]
    mask_list = []
    for step in range(WIN + 1):
        source = position - step
        usable = (step <= own_window) & (source >= 0)
        source_len = lengths[jnp.maximum(source, 0)]
        mask_list.append(usable & (token_ids < source_len))
    key_mask = jnp.concatenate(mask_list)
    all_keys = jnp.concatenate([p[0] for p in kv_list], axis=0)
    all_values = jnp.concatenate([p[1] for p in kv_list], axis=0)
    frame_parts = []
    for head_index in range(local_heads):
        lower = head_index * HD
        query_h = queries[:, lower : lower + HD]
        scores = lax.dot_general(
            query_h, all_keys[:, lower : lower + HD], (((1,), (1,)), ((), ())),
            preferred_element_type=jnp.float32) * scale
        scores = jnp.where(key_mask[None, :], scores, -jnp.inf)
        top_f = jnp.max(scores, axis=-1, keepdims=True)
        weights = jnp.exp(scores - top_f)
        total_f = jnp.sum(weights, axis=-1, keepdims=True)
        acc_f = jnp.dot(weights.astype(jnp.bfloat16), all_values[:, lower : lower + HD],
                        preferred_element_type=jnp.float32)
        frame_parts.append((top_f, total_f, acc_f))

    chips = lax.axis_size(CHIP_AXES)
    block = out_weight.shape[1]
    tokens = text_keys.shape[0]
    packed = jnp.concatenate([out_weight, text_keys.T, text_values.T], axis=1)
    packed = lax.all_gather(packed, CHIP_AXES, axis=1, tiled=True)
    packed, frame_parts = lax.optimization_barrier((packed, frame_parts))
    pair = jnp.stack([packed, swap_cores(packed)]).reshape(2, width, chips, -1)
    weight_pair = pair[:, :, :, :block]
    text_kt = pair[:, :, :, block : block + tokens].transpose(1, 0, 2, 3).reshape(width, -1)
    text_vt = pair[:, :, :, block + tokens :].transpose(1, 0, 2, 3).reshape(width, -1)

    head_outputs = []
    for head_index in range(local_heads):
        lower = head_index * HD
        query_h = queries[:, lower : lower + HD]
        top_f, total_f, acc_f = frame_parts[head_index]
        scores_t = jnp.dot(query_h, text_kt[lower : lower + HD], preferred_element_type=jnp.float32) * scale
        top_t = jnp.max(scores_t, axis=-1, keepdims=True)
        weights_t = jnp.exp(scores_t - top_t)
        total_t = jnp.sum(weights_t, axis=-1, keepdims=True)
        acc_t = lax.dot_general(
            weights_t.astype(jnp.bfloat16), text_vt[lower : lower + HD], (((1,), (1,)), ((), ())),
            preferred_element_type=jnp.float32)
        top = jnp.maximum(top_f, top_t)
        keep_f = jnp.exp(top_f - top)
        keep_t = jnp.exp(top_t - top)
        attended = (acc_f * keep_f + acc_t * keep_t) / (total_f * keep_f + total_t * keep_t)
        head_outputs.append(attended.astype(jnp.bfloat16))
    attended_all = jnp.concatenate(head_outputs, axis=1)
    ys = lax.axis_size("y")
    xs = lax.axis_size("x")
    w5 = weight_pair.reshape(2, width, ys, xs, block)
    partial_out = jnp.einsum("rk,ckyxn->yrcxn", attended_all, w5, preferred_element_type=jnp.float32)
    partial_out = partial_out.reshape(groups, rows, -1)
    mixed = lax.psum_scatter(partial_out.astype(jnp.bfloat16), "head", scatter_dimension=0, tiled=True)
    mixed = mixed.reshape(rows, 2, xs, block)
    mixed = jnp.where(first_core, mixed, mixed[:, ::-1])
    return mixed.transpose(0, 2, 1, 3).reshape(rows, -1)


def solution(mesh):
    frames, heads = mesh.devices.shape
    cores = 2
    xs = 4 if frames % (4 * cores) == 0 else 1
    grid = mesh.devices.reshape(frames // (xs * cores), xs, cores, heads)
    fine = jax.sharding.Mesh(grid, FRAME_AXES + ("head",))
    return jax.shard_map(
        on_device,
        mesh=fine,
        in_specs=(
            P(FRAME_AXES, "head"),
            P(FRAME_AXES, "head"),
            P(FRAME_AXES, "head"),
            P(FRAME_AXES, "head"),
            P(FRAME_AXES, "head"),
            P("head", FRAME_AXES),
            P(),
            P(),
        ),
        out_specs=P(FRAME_AXES, "head"),
        check_vma=False,
    )
```

```python
import math

import jax
import jax.numpy as jnp
from jax import lax
from jax.sharding import PartitionSpec as P

HD = 128
WIN = 4
FRAME_AXES = ("y", "x", "c")
CHIP_AXES = ("y", "x")


def shift_frames(value, steps):
    count = lax.axis_size(FRAME_AXES)
    return lax.ppermute(value, FRAME_AXES, [(source, source + steps) for source in range(count - steps)])


def relay_back(value, chips_back):
    ys, xs, cs = (lax.axis_size(name) for name in FRAME_AXES)
    count = ys * xs * cs
    first, second = [], []
    for y in range(ys):
        for x in range(xs):
            for c in range(cs):
                source = (y * xs + x) * cs + c
                middle = (y * xs + (x - 1) % xs) * cs + c
                first.append((source, middle))
                target = source + chips_back * cs
                if target < count:
                    second.append((middle, target))
    hop = lax.ppermute(value, FRAME_AXES, first)
    return lax.ppermute(hop, FRAME_AXES, second)


def swap_cores(value):
    return lax.ppermute(value, "c", [(0, 1), (1, 0)])


def on_device(queries, keys, values, text_keys, text_values, out_weight, windows, lengths):
    rows = queries.shape[0]
    width = queries.shape[1]
    local_heads = width // HD
    groups = lax.axis_size("head")
    scale = 1.0 / math.sqrt(HD)
    position = lax.axis_index(FRAME_AXES)
    core = lax.axis_index("c")
    first_core = core == 0

    own = jnp.stack([keys, values])
    back2 = shift_frames(own, 2)
    back4 = relay_back(own, 2)
    back1 = swap_cores(jnp.where(first_core, own, back2))
    back3 = swap_cores(jnp.where(first_core, back2, back4))
    kv_list = [own, back1, back2, back3, back4]

    token_ids = jnp.arange(rows, dtype=jnp.int32)
    own_window = windows[position]
    mask_list = []
    for step in range(WIN + 1):
        source = position - step
        usable = (step <= own_window) & (source >= 0)
        source_len = lengths[jnp.maximum(source, 0)]
        mask_list.append(usable & (token_ids < source_len))
    key_mask = jnp.concatenate(mask_list)
    all_keys = jnp.concatenate([p[0] for p in kv_list], axis=0)
    all_values = jnp.concatenate([p[1] for p in kv_list], axis=0)
    frame_parts = []
    for head_index in range(local_heads):
        lower = head_index * HD
        query_h = queries[:, lower : lower + HD]
        scores = lax.dot_general(
            query_h, all_keys[:, lower : lower + HD], (((1,), (1,)), ((), ())),
            preferred_element_type=jnp.float32) * scale
        scores = jnp.where(key_mask[None, :], scores, -jnp.inf)
        top_f = jnp.max(scores, axis=-1, keepdims=True)
        weights = jnp.exp(scores - top_f)
        total_f = jnp.sum(weights, axis=-1, keepdims=True)
        acc_f = jnp.dot(weights.astype(jnp.bfloat16), all_values[:, lower : lower + HD],
                        preferred_element_type=jnp.float32)
        frame_parts.append((top_f, total_f, acc_f))

    chips = lax.axis_size(CHIP_AXES)
    block = out_weight.shape[1]
    tokens = text_keys.shape[0]
    packed = jnp.concatenate([out_weight, text_keys.T, text_values.T], axis=1)
    packed = lax.all_gather(packed, CHIP_AXES, axis=1, tiled=True)
    packed, frame_parts = lax.optimization_barrier((packed, frame_parts))
    pair = jnp.stack([packed, swap_cores(packed)]).reshape(2, width, chips, -1)
    weight_pair = pair[:, :, :, :block]
    text_kt = pair[:, :, :, block : block + tokens].transpose(1, 0, 2, 3).reshape(width, -1)
    text_vt = pair[:, :, :, block + tokens :].transpose(1, 0, 2, 3).reshape(width, -1)

    head_outputs = []
    for head_index in range(local_heads):
        lower = head_index * HD
        query_h = queries[:, lower : lower + HD]
        top_f, total_f, acc_f = frame_parts[head_index]
        scores_t = jnp.dot(query_h, text_kt[lower : lower + HD], preferred_element_type=jnp.float32) * scale
        top_t = jnp.max(scores_t, axis=-1, keepdims=True)
        weights_t = jnp.exp(scores_t - top_t)
        total_t = jnp.sum(weights_t, axis=-1, keepdims=True)
        acc_t = lax.dot_general(
            weights_t.astype(jnp.bfloat16), text_vt[lower : lower + HD], (((1,), (1,)), ((), ())),
            preferred_element_type=jnp.float32)
        top = jnp.maximum(top_f, top_t)
        keep_f = jnp.exp(top_f - top)
        keep_t = jnp.exp(top_t - top)
        attended = (acc_f * keep_f + acc_t * keep_t) / (total_f * keep_f + total_t * keep_t)
        head_outputs.append(attended.astype(jnp.bfloat16))
    attended_all = jnp.concatenate(head_outputs, axis=1)
    ys = lax.axis_size("y")
    xs = lax.axis_size("x")
    w5 = weight_pair.reshape(2, width, ys, xs, block)
    partial_out = jnp.einsum("rk,ckyxn->yrcxn", attended_all, w5, preferred_element_type=jnp.float32)
    partial_out = partial_out.reshape(groups, rows, -1)
    mixed = lax.psum_scatter(partial_out.astype(jnp.bfloat16), "head", scatter_dimension=0, tiled=True)
    mixed = mixed.reshape(rows, 2, xs, block)
    mixed = jnp.where(first_core, mixed, mixed[:, ::-1])
    return mixed.transpose(0, 2, 1, 3).reshape(rows, -1)


def solution(mesh):
    frames, heads = mesh.devices.shape
    cores = 2
    xs = 4 if frames % (4 * cores) == 0 else 1
    grid = mesh.devices.reshape(frames // (xs * cores), xs, cores, heads)
    fine = jax.sharding.Mesh(grid, FRAME_AXES + ("head",))
    return jax.shard_map(
        on_device,
        mesh=fine,
        in_specs=(
            P(FRAME_AXES, "head"),
            P(FRAME_AXES, "head"),
            P(FRAME_AXES, "head"),
            P(FRAME_AXES, "head"),
            P(FRAME_AXES, "head"),
            P("head", FRAME_AXES),
            P(),
            P(),
        ),
        out_specs=P(FRAME_AXES, "head"),
        check_vma=False,
    )
```

```python
import math

import jax
import jax.numpy as jnp
from jax import lax
from jax.sharding import PartitionSpec as P

HD = 128
WIN = 4
FRAME_AXES = ("y", "x", "c")
CHIP_AXES = ("y", "x")
GATHER_SPARE = 8


def shift_frames(value, steps):
    count = lax.axis_size(FRAME_AXES)
    return lax.ppermute(value, FRAME_AXES, [(source, source + steps) for source in range(count - steps)])


def relay_back(value, chips_back):
    ys, xs, cs = (lax.axis_size(name) for name in FRAME_AXES)
    count = ys * xs * cs
    first, second = [], []
    for y in range(ys):
        for x in range(xs):
            for c in range(cs):
                source = (y * xs + x) * cs + c
                middle = (y * xs + (x - 1) % xs) * cs + c
                first.append((source, middle))
                target = source + chips_back * cs
                if target < count:
                    second.append((middle, target))
    hop = lax.ppermute(value, FRAME_AXES, first)
    return lax.ppermute(hop, FRAME_AXES, second)


def swap_cores(value):
    return lax.ppermute(value, "c", [(0, 1), (1, 0)])


def on_device(queries, keys, values, text_keys, text_values, out_weight, windows, lengths):
    rows = queries.shape[0]
    width = queries.shape[1]
    local_heads = width // HD
    groups = lax.axis_size("head")
    scale = 1.0 / math.sqrt(HD)
    position = lax.axis_index(FRAME_AXES)
    core = lax.axis_index("c")
    first_core = core == 0

    own = jnp.stack([keys, values])
    back2 = shift_frames(own, 2)
    back4 = relay_back(own, 2)
    back1 = swap_cores(jnp.where(first_core, own, back2))
    back3 = swap_cores(jnp.where(first_core, back2, back4))
    kv_list = [own, back1, back2, back3, back4]

    token_ids = jnp.arange(rows, dtype=jnp.int32)
    own_window = windows[position]
    mask_list = []
    for step in range(WIN + 1):
        source = position - step
        usable = (step <= own_window) & (source >= 0)
        source_len = lengths[jnp.maximum(source, 0)]
        mask_list.append(usable & (token_ids < source_len))
    key_mask = jnp.concatenate(mask_list)
    all_keys = jnp.concatenate([p[0] for p in kv_list], axis=0)
    all_values = jnp.concatenate([p[1] for p in kv_list], axis=0)
    frame_parts = []
    for head_index in range(local_heads):
        lower = head_index * HD
        query_h = queries[:, lower : lower + HD]
        scores = lax.dot_general(
            query_h, all_keys[:, lower : lower + HD], (((1,), (1,)), ((), ())),
            preferred_element_type=jnp.float32) * scale
        scores = jnp.where(key_mask[None, :], scores, -jnp.inf)
        top_f = jnp.max(scores, axis=-1, keepdims=True)
        weights = jnp.exp(scores - top_f)
        total_f = jnp.sum(weights, axis=-1, keepdims=True)
        acc_f = jnp.dot(weights.astype(jnp.bfloat16), all_values[:, lower : lower + HD],
                        preferred_element_type=jnp.float32)
        frame_parts.append((top_f, total_f, acc_f))

    chips = lax.axis_size(CHIP_AXES)
    block = out_weight.shape[1]
    tokens = text_keys.shape[0]
    spare = jnp.zeros((width, GATHER_SPARE), out_weight.dtype)
    packed = jnp.concatenate([out_weight, text_keys.T, text_values.T, spare], axis=1)
    packed = lax.all_gather(lax.all_gather(packed, "y", axis=1, tiled=True), "x", axis=1, tiled=True)
    packed, frame_parts = lax.optimization_barrier((packed, frame_parts))
    pair = jnp.stack([packed, swap_cores(packed)]).reshape(2, width, chips, -1)
    weight_pair = pair[:, :, :, :block]
    text_kt = pair[:, :, :, block : block + tokens].transpose(1, 0, 2, 3).reshape(width, -1)
    text_vt = pair[:, :, :, block + tokens : block + 2 * tokens].transpose(1, 0, 2, 3).reshape(width, -1)

    head_outputs = []
    for head_index in range(local_heads):
        lower = head_index * HD
        query_h = queries[:, lower : lower + HD]
        top_f, total_f, acc_f = frame_parts[head_index]
        scores_t = jnp.dot(query_h, text_kt[lower : lower + HD], preferred_element_type=jnp.float32) * scale
        top_t = jnp.max(scores_t, axis=-1, keepdims=True)
        weights_t = jnp.exp(scores_t - top_t)
        total_t = jnp.sum(weights_t, axis=-1, keepdims=True)
        acc_t = lax.dot_general(
            weights_t.astype(jnp.bfloat16), text_vt[lower : lower + HD], (((1,), (1,)), ((), ())),
            preferred_element_type=jnp.float32)
        top = jnp.maximum(top_f, top_t)
        keep_f = jnp.exp(top_f - top)
        keep_t = jnp.exp(top_t - top)
        attended = (acc_f * keep_f + acc_t * keep_t) / (total_f * keep_f + total_t * keep_t)
        head_outputs.append(attended.astype(jnp.bfloat16))
    attended_all = jnp.concatenate(head_outputs, axis=1)
    ys = lax.axis_size("y")
    xs = lax.axis_size("x")
    w5 = weight_pair.reshape(2, width, xs, ys, block)
    partial_out = jnp.einsum("rk,ckxyn->yrcxn", attended_all, w5, preferred_element_type=jnp.float32)
    partial_out = partial_out.reshape(groups, rows, -1)
    mixed = lax.psum_scatter(partial_out.astype(jnp.bfloat16), "head", scatter_dimension=0, tiled=True)
    mixed = mixed.reshape(rows, 2, xs, block)
    mixed = jnp.where(first_core, mixed, mixed[:, ::-1])
    return mixed.transpose(0, 2, 1, 3).reshape(rows, -1)


def solution(mesh):
    frames, heads = mesh.devices.shape
    cores = 2
    xs = 4 if frames % (4 * cores) == 0 else 1
    grid = mesh.devices.reshape(frames // (xs * cores), xs, cores, heads)
    fine = jax.sharding.Mesh(grid, FRAME_AXES + ("head",))
    return jax.shard_map(
        on_device,
        mesh=fine,
        in_specs=(
            P(FRAME_AXES, "head"),
            P(FRAME_AXES, "head"),
            P(FRAME_AXES, "head"),
            P(FRAME_AXES, "head"),
            P(FRAME_AXES, "head"),
            P("head", FRAME_AXES),
            P(),
            P(),
        ),
        out_specs=P(FRAME_AXES, "head"),
        check_vma=False,
    )
```

```python
import math

import jax
import jax.numpy as jnp
from jax import lax
from jax.sharding import PartitionSpec as P

HD = 128
WIN = 4
FRAME_AXES = ("y", "x", "c")
CHIP_AXES = ("y", "x")
GATHER_SPARE = 8


def shift_frames(value, steps):
    count = lax.axis_size(FRAME_AXES)
    return lax.ppermute(value, FRAME_AXES, [(source, source + steps) for source in range(count - steps)])


def relay_back(value, chips_back):
    ys, xs, cs = (lax.axis_size(name) for name in FRAME_AXES)
    count = ys * xs * cs
    first, second = [], []
    for y in range(ys):
        for x in range(xs):
            for c in range(cs):
                source = (y * xs + x) * cs + c
                middle = (y * xs + (x - 1) % xs) * cs + c
                first.append((source, middle))
                target = source + chips_back * cs
                if target < count:
                    second.append((middle, target))
    hop = lax.ppermute(value, FRAME_AXES, first)
    return lax.ppermute(hop, FRAME_AXES, second)


def swap_cores(value):
    return lax.ppermute(value, "c", [(0, 1), (1, 0)])


def on_device(queries, keys, values, text_keys, text_values, out_weight, windows, lengths):
    rows = queries.shape[0]
    width = queries.shape[1]
    local_heads = width // HD
    groups = lax.axis_size("head")
    scale = 1.0 / math.sqrt(HD)
    position = lax.axis_index(FRAME_AXES)
    core = lax.axis_index("c")
    first_core = core == 0

    own = jnp.stack([keys, values])
    back2 = shift_frames(own, 2)
    back4 = relay_back(own, 2)
    back1 = swap_cores(jnp.where(first_core, own, back2))
    back3 = swap_cores(jnp.where(first_core, back2, back4))
    kv_list = [own, back1, back2, back3, back4]

    token_ids = jnp.arange(rows, dtype=jnp.int32)
    own_window = windows[position]
    mask_list = []
    for step in range(WIN + 1):
        source = position - step
        usable = (step <= own_window) & (source >= 0)
        source_len = lengths[jnp.maximum(source, 0)]
        mask_list.append(usable & (token_ids < source_len))
    key_mask = jnp.concatenate(mask_list)
    all_keys = jnp.concatenate([p[0] for p in kv_list], axis=0)
    all_values = jnp.concatenate([p[1] for p in kv_list], axis=0)
    frame_parts = []
    for head_index in range(local_heads):
        lower = head_index * HD
        query_h = queries[:, lower : lower + HD]
        scores = lax.dot_general(
            query_h, all_keys[:, lower : lower + HD], (((1,), (1,)), ((), ())),
            preferred_element_type=jnp.float32) * scale
        scores = jnp.where(key_mask[None, :], scores, -jnp.inf)
        top_f = jnp.max(scores, axis=-1, keepdims=True)
        weights = jnp.exp(scores - top_f)
        total_f = jnp.sum(weights, axis=-1, keepdims=True)
        acc_f = jnp.dot(weights.astype(jnp.bfloat16), all_values[:, lower : lower + HD],
                        preferred_element_type=jnp.float32)
        frame_parts.append((top_f, total_f, acc_f))

    chips = lax.axis_size(CHIP_AXES)
    block = out_weight.shape[1]
    tokens = text_keys.shape[0]
    spare = jnp.zeros((width, GATHER_SPARE), out_weight.dtype)
    packed = jnp.concatenate([out_weight, text_keys.T, text_values.T, spare], axis=1)
    packed = lax.all_gather(lax.all_gather(packed, "y", axis=1, tiled=True), "x", axis=1, tiled=True)
    packed, frame_parts = lax.optimization_barrier((packed, frame_parts))
    packed = packed.reshape(width, chips, -1)
    text_own = packed[:, :, block : block + 2 * tokens]
    text_pair = jnp.stack([text_own, swap_cores(text_own)])
    text_kt = text_pair[:, :, :, :tokens].transpose(1, 0, 2, 3).reshape(width, -1)
    text_vt = text_pair[:, :, :, tokens:].transpose(1, 0, 2, 3).reshape(width, -1)
    weight_own = packed[:, :, :block]
    weight_pair = jnp.stack([weight_own, swap_cores(weight_own)])

    head_outputs = []
    for head_index in range(local_heads):
        lower = head_index * HD
        query_h = queries[:, lower : lower + HD]
        top_f, total_f, acc_f = frame_parts[head_index]
        scores_t = jnp.dot(query_h, text_kt[lower : lower + HD], preferred_element_type=jnp.float32) * scale
        top_t = jnp.max(scores_t, axis=-1, keepdims=True)
        weights_t = jnp.exp(scores_t - top_t)
        total_t = jnp.sum(weights_t, axis=-1, keepdims=True)
        acc_t = lax.dot_general(
            weights_t.astype(jnp.bfloat16), text_vt[lower : lower + HD], (((1,), (1,)), ((), ())),
            preferred_element_type=jnp.float32)
        top = jnp.maximum(top_f, top_t)
        keep_f = jnp.exp(top_f - top)
        keep_t = jnp.exp(top_t - top)
        attended = (acc_f * keep_f + acc_t * keep_t) / (total_f * keep_f + total_t * keep_t)
        head_outputs.append(attended.astype(jnp.bfloat16))
    attended_all = jnp.concatenate(head_outputs, axis=1)
    ys = lax.axis_size("y")
    xs = lax.axis_size("x")
    w5 = weight_pair.reshape(2, width, xs, ys, block)
    partial_out = jnp.einsum("rk,ckxyn->yrcxn", attended_all, w5, preferred_element_type=jnp.float32)
    partial_out = partial_out.reshape(groups, rows, -1)
    mixed = lax.psum_scatter(partial_out.astype(jnp.bfloat16), "head", scatter_dimension=0, tiled=True)
    mixed = mixed.reshape(rows, 2, xs, block)
    mixed = jnp.where(first_core, mixed, mixed[:, ::-1])
    return mixed.transpose(0, 2, 1, 3).reshape(rows, -1)


def solution(mesh):
    frames, heads = mesh.devices.shape
    cores = 2
    xs = 4 if frames % (4 * cores) == 0 else 1
    grid = mesh.devices.reshape(frames // (xs * cores), xs, cores, heads)
    fine = jax.sharding.Mesh(grid, FRAME_AXES + ("head",))
    return jax.shard_map(
        on_device,
        mesh=fine,
        in_specs=(
            P(FRAME_AXES, "head"),
            P(FRAME_AXES, "head"),
            P(FRAME_AXES, "head"),
            P(FRAME_AXES, "head"),
            P(FRAME_AXES, "head"),
            P("head", FRAME_AXES),
            P(),
            P(),
        ),
        out_specs=P(FRAME_AXES, "head"),
        check_vma=False,
    )
```

```python
import math

import jax
import jax.numpy as jnp
from jax import lax
from jax.sharding import PartitionSpec as P

HD = 128
WIN = 4
FRAME_AXES = ("y", "x", "c")
CHIP_AXES = ("y", "x")
GATHER_SPARE = 8


def shift_frames(value, steps):
    count = lax.axis_size(FRAME_AXES)
    return lax.ppermute(value, FRAME_AXES, [(source, source + steps) for source in range(count - steps)])


def relay_back(value, chips_back):
    ys, xs, cs = (lax.axis_size(name) for name in FRAME_AXES)
    count = ys * xs * cs
    first, second = [], []
    for y in range(ys):
        for x in range(xs):
            for c in range(cs):
                source = (y * xs + x) * cs + c
                middle = (y * xs + (x - 1) % xs) * cs + c
                first.append((source, middle))
                target = source + chips_back * cs
                if target < count:
                    second.append((middle, target))
    hop = lax.ppermute(value, FRAME_AXES, first)
    return lax.ppermute(hop, FRAME_AXES, second)


def swap_cores(value):
    return lax.ppermute(value, "c", [(0, 1), (1, 0)])


def on_device(queries, keys, values, text_keys, text_values, out_weight, windows, lengths):
    rows = queries.shape[0]
    width = queries.shape[1]
    local_heads = width // HD
    groups = lax.axis_size("head")
    scale = 1.0 / math.sqrt(HD)
    position = lax.axis_index(FRAME_AXES)
    core = lax.axis_index("c")
    first_core = core == 0

    own = jnp.stack([keys, values])
    back2 = shift_frames(own, 2)
    back4 = relay_back(own, 2)
    back1, back3 = swap_cores(jnp.where(first_core, jnp.stack([own, back2]), jnp.stack([back2, back4])))
    kv_list = [own, back1, back2, back3, back4]

    token_ids = jnp.arange(rows, dtype=jnp.int32)
    own_window = windows[position]
    mask_list = []
    for step in range(WIN + 1):
        source = position - step
        usable = (step <= own_window) & (source >= 0)
        source_len = lengths[jnp.maximum(source, 0)]
        mask_list.append(usable & (token_ids < source_len))
    key_mask = jnp.concatenate(mask_list)
    all_keys = jnp.concatenate([p[0] for p in kv_list], axis=0)
    all_values = jnp.concatenate([p[1] for p in kv_list], axis=0)
    frame_parts = []
    for head_index in range(local_heads):
        lower = head_index * HD
        query_h = queries[:, lower : lower + HD]
        scores = lax.dot_general(
            query_h, all_keys[:, lower : lower + HD], (((1,), (1,)), ((), ())),
            preferred_element_type=jnp.float32) * scale
        scores = jnp.where(key_mask[None, :], scores, -jnp.inf)
        top_f = jnp.max(scores, axis=-1, keepdims=True)
        weights = jnp.exp(scores - top_f)
        total_f = jnp.sum(weights, axis=-1, keepdims=True)
        acc_f = jnp.dot(weights.astype(jnp.bfloat16), all_values[:, lower : lower + HD],
                        preferred_element_type=jnp.float32)
        frame_parts.append((top_f, total_f, acc_f))

    chips = lax.axis_size(CHIP_AXES)
    block = out_weight.shape[1]
    tokens = text_keys.shape[0]
    spare = jnp.zeros((width, GATHER_SPARE), out_weight.dtype)
    packed = jnp.concatenate([out_weight, text_keys.T, text_values.T, spare], axis=1)
    packed = lax.all_gather(lax.all_gather(packed, "y", axis=1, tiled=True), "x", axis=1, tiled=True)
    packed, frame_parts = lax.optimization_barrier((packed, frame_parts))
    packed = packed.reshape(width, chips, -1)
    text_own = packed[:, :, block : block + 2 * tokens]
    text_pair = jnp.stack([text_own, swap_cores(text_own)])
    text_kt = text_pair[:, :, :, :tokens].transpose(1, 0, 2, 3).reshape(width, -1)
    text_vt = text_pair[:, :, :, tokens:].transpose(1, 0, 2, 3).reshape(width, -1)
    weight_own = packed[:, :, :block]
    weight_pair = jnp.stack([weight_own, swap_cores(weight_own)])

    head_outputs = []
    for head_index in range(local_heads):
        lower = head_index * HD
        query_h = queries[:, lower : lower + HD]
        top_f, total_f, acc_f = frame_parts[head_index]
        scores_t = jnp.dot(query_h, text_kt[lower : lower + HD], preferred_element_type=jnp.float32) * scale
        top_t = jnp.max(scores_t, axis=-1, keepdims=True)
        weights_t = jnp.exp(scores_t - top_t)
        total_t = jnp.sum(weights_t, axis=-1, keepdims=True)
        acc_t = lax.dot_general(
            weights_t.astype(jnp.bfloat16), text_vt[lower : lower + HD], (((1,), (1,)), ((), ())),
            preferred_element_type=jnp.float32)
        top = jnp.maximum(top_f, top_t)
        keep_f = jnp.exp(top_f - top)
        keep_t = jnp.exp(top_t - top)
        attended = (acc_f * keep_f + acc_t * keep_t) / (total_f * keep_f + total_t * keep_t)
        head_outputs.append(attended.astype(jnp.bfloat16))
    attended_all = jnp.concatenate(head_outputs, axis=1)
    ys = lax.axis_size("y")
    xs = lax.axis_size("x")
    w5 = weight_pair.reshape(2, width, xs, ys, block)
    partial_out = jnp.einsum("rk,ckxyn->yrcxn", attended_all, w5, preferred_element_type=jnp.float32)
    partial_out = partial_out.reshape(groups, rows, -1)
    mixed = lax.psum_scatter(partial_out.astype(jnp.bfloat16), "head", scatter_dimension=0, tiled=True)
    mixed = mixed.reshape(rows, 2, xs, block)
    mixed = jnp.where(first_core, mixed, mixed[:, ::-1])
    return mixed.transpose(0, 2, 1, 3).reshape(rows, -1)


def solution(mesh):
    frames, heads = mesh.devices.shape
    cores = 2
    xs = 4 if frames % (4 * cores) == 0 else 1
    grid = mesh.devices.reshape(frames // (xs * cores), xs, cores, heads)
    fine = jax.sharding.Mesh(grid, FRAME_AXES + ("head",))
    return jax.shard_map(
        on_device,
        mesh=fine,
        in_specs=(
            P(FRAME_AXES, "head"),
            P(FRAME_AXES, "head"),
            P(FRAME_AXES, "head"),
            P(FRAME_AXES, "head"),
            P(FRAME_AXES, "head"),
            P("head", FRAME_AXES),
            P(),
            P(),
        ),
        out_specs=P(FRAME_AXES, "head"),
        check_vma=False,
    )
```

```python
import math

import jax
import jax.numpy as jnp
from jax import lax
from jax.sharding import PartitionSpec as P

HD = 128
WIN = 4
FRAME_AXES = ("y", "x", "c")
CHIP_AXES = ("y", "x")
GATHER_SPARE = 8


def shift_frames(value, steps):
    count = lax.axis_size(FRAME_AXES)
    return lax.ppermute(value, FRAME_AXES, [(source, source + steps) for source in range(count - steps)])


def relay_back(value, chips_back):
    ys, xs, cs = (lax.axis_size(name) for name in FRAME_AXES)
    count = ys * xs * cs
    first, second = [], []
    for y in range(ys):
        for x in range(xs):
            for c in range(cs):
                source = (y * xs + x) * cs + c
                middle = (y * xs + (x - 1) % xs) * cs + c
                first.append((source, middle))
                target = source + chips_back * cs
                if target < count:
                    second.append((middle, target))
    hop = lax.ppermute(value, FRAME_AXES, first)
    return lax.ppermute(hop, FRAME_AXES, second)


def swap_cores(value):
    return lax.ppermute(value, "c", [(0, 1), (1, 0)])


def on_device(queries, keys, values, text_keys, text_values, out_weight, windows, lengths):
    rows = queries.shape[0]
    width = queries.shape[1]
    local_heads = width // HD
    groups = lax.axis_size("head")
    scale = 1.0 / math.sqrt(HD)
    position = lax.axis_index(FRAME_AXES)
    core = lax.axis_index("c")
    first_core = core == 0

    own = jnp.stack([keys, values])
    back2 = shift_frames(own, 2)
    back4 = relay_back(own, 2)
    back1 = swap_cores(jnp.where(first_core, own, back2))
    back3 = swap_cores(jnp.where(first_core, back2, back4))
    kv_list = [own, back1, back2, back3, back4]

    token_ids = jnp.arange(rows, dtype=jnp.int32)
    own_window = windows[position]
    mask_list = []
    for step in range(WIN + 1):
        source = position - step
        usable = (step <= own_window) & (source >= 0)
        source_len = lengths[jnp.maximum(source, 0)]
        mask_list.append(usable & (token_ids < source_len))
    key_mask = jnp.concatenate(mask_list)
    all_keys = jnp.concatenate([p[0] for p in kv_list], axis=0)
    all_values = jnp.concatenate([p[1] for p in kv_list], axis=0)
    frame_parts = []
    for head_index in range(local_heads):
        lower = head_index * HD
        query_h = queries[:, lower : lower + HD]
        scores = lax.dot_general(
            query_h, all_keys[:, lower : lower + HD], (((1,), (1,)), ((), ())),
            preferred_element_type=jnp.float32) * scale
        scores = jnp.where(key_mask[None, :], scores, -jnp.inf)
        top_f = jnp.max(scores, axis=-1, keepdims=True)
        weights = jnp.exp(scores - top_f)
        total_f = jnp.sum(weights, axis=-1, keepdims=True)
        acc_f = jnp.dot(weights.astype(jnp.bfloat16), all_values[:, lower : lower + HD],
                        preferred_element_type=jnp.float32)
        frame_parts.append((top_f, total_f, acc_f))

    chips = lax.axis_size(CHIP_AXES)
    block = out_weight.shape[1]
    tokens = text_keys.shape[0]
    spare = jnp.zeros((width, GATHER_SPARE), out_weight.dtype)
    packed = jnp.concatenate([out_weight, text_keys.T, text_values.T, spare], axis=1)
    packed = lax.all_gather(lax.all_gather(packed, "x", axis=1, tiled=True), "y", axis=1, tiled=True)
    packed, frame_parts = lax.optimization_barrier((packed, frame_parts))
    packed = packed.reshape(width, chips, -1)
    text_own = packed[:, :, block : block + 2 * tokens]
    text_pair = jnp.stack([text_own, swap_cores(text_own)])
    text_kt = text_pair[:, :, :, :tokens].transpose(1, 0, 2, 3).reshape(width, -1)
    text_vt = text_pair[:, :, :, tokens:].transpose(1, 0, 2, 3).reshape(width, -1)
    weight_own = packed[:, :, :block]
    weight_pair = jnp.stack([weight_own, swap_cores(weight_own)])

    head_outputs = []
    for head_index in range(local_heads):
        lower = head_index * HD
        query_h = queries[:, lower : lower + HD]
        top_f, total_f, acc_f = frame_parts[head_index]
        scores_t = jnp.dot(query_h, text_kt[lower : lower + HD], preferred_element_type=jnp.float32) * scale
        top_t = jnp.max(scores_t, axis=-1, keepdims=True)
        weights_t = jnp.exp(scores_t - top_t)
        total_t = jnp.sum(weights_t, axis=-1, keepdims=True)
        acc_t = lax.dot_general(
            weights_t.astype(jnp.bfloat16), text_vt[lower : lower + HD], (((1,), (1,)), ((), ())),
            preferred_element_type=jnp.float32)
        top = jnp.maximum(top_f, top_t)
        keep_f = jnp.exp(top_f - top)
        keep_t = jnp.exp(top_t - top)
        attended = (acc_f * keep_f + acc_t * keep_t) / (total_f * keep_f + total_t * keep_t)
        head_outputs.append(attended.astype(jnp.bfloat16))
    attended_all = jnp.concatenate(head_outputs, axis=1)
    ys = lax.axis_size("y")
    xs = lax.axis_size("x")
    w5 = weight_pair.reshape(2, width, ys, xs, block)
    partial_out = jnp.einsum("rk,ckyxn->yrcxn", attended_all, w5, preferred_element_type=jnp.float32)
    partial_out = partial_out.reshape(groups, rows, -1)
    mixed = lax.psum_scatter(partial_out.astype(jnp.bfloat16), "head", scatter_dimension=0, tiled=True)
    mixed = mixed.reshape(rows, 2, xs, block)
    mixed = jnp.where(first_core, mixed, mixed[:, ::-1])
    return mixed.transpose(0, 2, 1, 3).reshape(rows, -1)


def solution(mesh):
    frames, heads = mesh.devices.shape
    cores = 2
    xs = 4 if frames % (4 * cores) == 0 else 1
    grid = mesh.devices.reshape(frames // (xs * cores), xs, cores, heads)
    fine = jax.sharding.Mesh(grid, FRAME_AXES + ("head",))
    return jax.shard_map(
        on_device,
        mesh=fine,
        in_specs=(
            P(FRAME_AXES, "head"),
            P(FRAME_AXES, "head"),
            P(FRAME_AXES, "head"),
            P(FRAME_AXES, "head"),
            P(FRAME_AXES, "head"),
            P("head", FRAME_AXES),
            P(),
            P(),
        ),
        out_specs=P(FRAME_AXES, "head"),
        check_vma=False,
    )
```

```python
import math

import jax
import jax.numpy as jnp
from jax import lax
from jax.sharding import PartitionSpec as P

HD = 128
WIN = 4
FRAME_AXES = ("y", "x", "c")
CHIP_AXES = ("y", "x")
GATHER_SPARE = 8


def shift_frames(value, steps):
    count = lax.axis_size(FRAME_AXES)
    return lax.ppermute(value, FRAME_AXES, [(source, source + steps) for source in range(count - steps)])


def relay_back(value, chips_back):
    ys, xs, cs = (lax.axis_size(name) for name in FRAME_AXES)
    count = ys * xs * cs
    first, second = [], []
    for y in range(ys):
        for x in range(xs):
            for c in range(cs):
                source = (y * xs + x) * cs + c
                middle = (y * xs + (x - 1) % xs) * cs + c
                first.append((source, middle))
                target = source + chips_back * cs
                if target < count:
                    second.append((middle, target))
    hop = lax.ppermute(value, FRAME_AXES, first)
    return lax.ppermute(hop, FRAME_AXES, second)


def swap_cores(value):
    return lax.ppermute(value, "c", [(0, 1), (1, 0)])


def on_device(queries, keys, values, text_keys, text_values, out_weight, windows, lengths):
    rows = queries.shape[0]
    width = queries.shape[1]
    local_heads = width // HD
    groups = lax.axis_size("head")
    scale = 1.0 / math.sqrt(HD)
    position = lax.axis_index(FRAME_AXES)
    core = lax.axis_index("c")
    first_core = core == 0

    own = jnp.stack([keys, values])
    back2 = shift_frames(own, 2)
    back4 = relay_back(own, 2)
    back1 = swap_cores(jnp.where(first_core, own, back2))
    back3 = swap_cores(jnp.where(first_core, back2, back4))
    kv_list = [own, back1, back2, back3, back4]

    token_ids = jnp.arange(rows, dtype=jnp.int32)
    own_window = windows[position]
    mask_list = []
    for step in range(WIN + 1):
        source = position - step
        usable = (step <= own_window) & (source >= 0)
        source_len = lengths[jnp.maximum(source, 0)]
        mask_list.append(usable & (token_ids < source_len))
    key_mask = jnp.concatenate(mask_list)
    all_keys = jnp.concatenate([p[0] for p in kv_list], axis=0)
    all_values = jnp.concatenate([p[1] for p in kv_list], axis=0)
    frame_parts = []
    for head_index in range(local_heads):
        lower = head_index * HD
        query_h = queries[:, lower : lower + HD]
        scores = lax.dot_general(
            query_h, all_keys[:, lower : lower + HD], (((1,), (1,)), ((), ())),
            preferred_element_type=jnp.float32) * scale
        scores = jnp.where(key_mask[None, :], scores, -jnp.inf)
        top_f = jnp.max(scores, axis=-1, keepdims=True)
        weights = jnp.exp(scores - top_f)
        total_f = jnp.sum(weights, axis=-1, keepdims=True)
        acc_f = jnp.dot(weights.astype(jnp.bfloat16), all_values[:, lower : lower + HD],
                        preferred_element_type=jnp.float32)
        frame_parts.append((top_f, total_f, acc_f))

    chips = lax.axis_size(CHIP_AXES)
    block = out_weight.shape[1]
    tokens = text_keys.shape[0]
    spare = jnp.zeros((width, GATHER_SPARE), out_weight.dtype)
    packed = jnp.concatenate([out_weight, text_keys.T, text_values.T, spare], axis=1)
    packed = lax.all_gather(packed, "y", axis=1, tiled=True).reshape(width, lax.axis_size("y"), -1)
    packed = packed[:, :, : block + 2 * tokens].reshape(width, -1)
    packed = lax.all_gather(packed, "x", axis=1, tiled=True)
    packed, frame_parts = lax.optimization_barrier((packed, frame_parts))
    packed = packed.reshape(width, chips, -1)
    text_own = packed[:, :, block : block + 2 * tokens]
    text_pair = jnp.stack([text_own, swap_cores(text_own)])
    text_kt = text_pair[:, :, :, :tokens].transpose(1, 0, 2, 3).reshape(width, -1)
    text_vt = text_pair[:, :, :, tokens:].transpose(1, 0, 2, 3).reshape(width, -1)
    weight_own = packed[:, :, :block]
    weight_pair = jnp.stack([weight_own, swap_cores(weight_own)])

    head_outputs = []
    for head_index in range(local_heads):
        lower = head_index * HD
        query_h = queries[:, lower : lower + HD]
        top_f, total_f, acc_f = frame_parts[head_index]
        scores_t = jnp.dot(query_h, text_kt[lower : lower + HD], preferred_element_type=jnp.float32) * scale
        top_t = jnp.max(scores_t, axis=-1, keepdims=True)
        weights_t = jnp.exp(scores_t - top_t)
        total_t = jnp.sum(weights_t, axis=-1, keepdims=True)
        acc_t = lax.dot_general(
            weights_t.astype(jnp.bfloat16), text_vt[lower : lower + HD], (((1,), (1,)), ((), ())),
            preferred_element_type=jnp.float32)
        top = jnp.maximum(top_f, top_t)
        keep_f = jnp.exp(top_f - top)
        keep_t = jnp.exp(top_t - top)
        attended = (acc_f * keep_f + acc_t * keep_t) / (total_f * keep_f + total_t * keep_t)
        head_outputs.append(attended.astype(jnp.bfloat16))
    attended_all = jnp.concatenate(head_outputs, axis=1)
    ys = lax.axis_size("y")
    xs = lax.axis_size("x")
    w5 = weight_pair.reshape(2, width, xs, ys, block)
    partial_out = jnp.einsum("rk,ckxyn->yrcxn", attended_all, w5, preferred_element_type=jnp.float32)
    partial_out = partial_out.reshape(groups, rows, -1)
    mixed = lax.psum_scatter(partial_out.astype(jnp.bfloat16), "head", scatter_dimension=0, tiled=True)
    mixed = mixed.reshape(rows, 2, xs, block)
    mixed = jnp.where(first_core, mixed, mixed[:, ::-1])
    return mixed.transpose(0, 2, 1, 3).reshape(rows, -1)


def solution(mesh):
    frames, heads = mesh.devices.shape
    cores = 2
    xs = 4 if frames % (4 * cores) == 0 else 1
    grid = mesh.devices.reshape(frames // (xs * cores), xs, cores, heads)
    fine = jax.sharding.Mesh(grid, FRAME_AXES + ("head",))
    return jax.shard_map(
        on_device,
        mesh=fine,
        in_specs=(
            P(FRAME_AXES, "head"),
            P(FRAME_AXES, "head"),
            P(FRAME_AXES, "head"),
            P(FRAME_AXES, "head"),
            P(FRAME_AXES, "head"),
            P("head", FRAME_AXES),
            P(),
            P(),
        ),
        out_specs=P(FRAME_AXES, "head"),
        check_vma=False,
    )
```

```python
import math

import jax
import jax.numpy as jnp
from jax import lax
from jax.sharding import PartitionSpec as P

HD = 128
WIN = 4
FRAME_AXES = ("y", "x", "c")
CHIP_AXES = ("y", "x")
GATHER_SPARE = 8


def shift_frames(value, steps):
    count = lax.axis_size(FRAME_AXES)
    return lax.ppermute(value, FRAME_AXES, [(source, source + steps) for source in range(count - steps)])


def relay_back(value, chips_back):
    ys, xs, cs = (lax.axis_size(name) for name in FRAME_AXES)
    count = ys * xs * cs
    first, second = [], []
    for y in range(ys):
        for x in range(xs):
            for c in range(cs):
                source = (y * xs + x) * cs + c
                middle = (y * xs + (x - 1) % xs) * cs + c
                first.append((source, middle))
                target = source + chips_back * cs
                if target < count:
                    second.append((middle, target))
    hop = lax.ppermute(value, FRAME_AXES, first)
    return lax.ppermute(hop, FRAME_AXES, second)


def swap_cores(value):
    return lax.ppermute(value, "c", [(0, 1), (1, 0)])


def on_device(queries, keys, values, text_keys, text_values, out_weight, windows, lengths):
    rows = queries.shape[0]
    width = queries.shape[1]
    local_heads = width // HD
    groups = lax.axis_size("head")
    scale = 1.0 / math.sqrt(HD)
    position = lax.axis_index(FRAME_AXES)
    core = lax.axis_index("c")
    first_core = core == 0

    chips = lax.axis_size(CHIP_AXES)
    block = out_weight.shape[1]
    tokens = text_keys.shape[0]
    spare = jnp.zeros((width, GATHER_SPARE), out_weight.dtype)
    packed = jnp.concatenate([out_weight, text_keys.T, text_values.T, spare], axis=1)
    packed, keys, values = lax.optimization_barrier((packed, keys, values))
    packed = lax.all_gather(lax.all_gather(packed, "y", axis=1, tiled=True), "x", axis=1, tiled=True)
    own = jnp.stack([keys, values])
    back2 = shift_frames(own, 2)
    back4 = relay_back(own, 2)
    back1 = swap_cores(jnp.where(first_core, own, back2))
    back3 = swap_cores(jnp.where(first_core, back2, back4))
    kv_list = [own, back1, back2, back3, back4]

    token_ids = jnp.arange(rows, dtype=jnp.int32)
    own_window = windows[position]
    mask_list = []
    for step in range(WIN + 1):
        source = position - step
        usable = (step <= own_window) & (source >= 0)
        source_len = lengths[jnp.maximum(source, 0)]
        mask_list.append(usable & (token_ids < source_len))
    key_mask = jnp.concatenate(mask_list)
    all_keys = jnp.concatenate([p[0] for p in kv_list], axis=0)
    all_values = jnp.concatenate([p[1] for p in kv_list], axis=0)
    frame_parts = []
    for head_index in range(local_heads):
        lower = head_index * HD
        query_h = queries[:, lower : lower + HD]
        scores = lax.dot_general(
            query_h, all_keys[:, lower : lower + HD], (((1,), (1,)), ((), ())),
            preferred_element_type=jnp.float32) * scale
        scores = jnp.where(key_mask[None, :], scores, -jnp.inf)
        top_f = jnp.max(scores, axis=-1, keepdims=True)
        weights = jnp.exp(scores - top_f)
        total_f = jnp.sum(weights, axis=-1, keepdims=True)
        acc_f = jnp.dot(weights.astype(jnp.bfloat16), all_values[:, lower : lower + HD],
                        preferred_element_type=jnp.float32)
        frame_parts.append((top_f, total_f, acc_f))

    packed, frame_parts = lax.optimization_barrier((packed, frame_parts))
    packed = packed.reshape(width, chips, -1)
    text_own = packed[:, :, block : block + 2 * tokens]
    text_pair = jnp.stack([text_own, swap_cores(text_own)])
    text_kt = text_pair[:, :, :, :tokens].transpose(1, 0, 2, 3).reshape(width, -1)
    text_vt = text_pair[:, :, :, tokens:].transpose(1, 0, 2, 3).reshape(width, -1)
    weight_own = packed[:, :, :block]
    weight_pair = jnp.stack([weight_own, swap_cores(weight_own)])

    head_outputs = []
    for head_index in range(local_heads):
        lower = head_index * HD
        query_h = queries[:, lower : lower + HD]
        top_f, total_f, acc_f = frame_parts[head_index]
        scores_t = jnp.dot(query_h, text_kt[lower : lower + HD], preferred_element_type=jnp.float32) * scale
        top_t = jnp.max(scores_t, axis=-1, keepdims=True)
        weights_t = jnp.exp(scores_t - top_t)
        total_t = jnp.sum(weights_t, axis=-1, keepdims=True)
        acc_t = lax.dot_general(
            weights_t.astype(jnp.bfloat16), text_vt[lower : lower + HD], (((1,), (1,)), ((), ())),
            preferred_element_type=jnp.float32)
        top = jnp.maximum(top_f, top_t)
        keep_f = jnp.exp(top_f - top)
        keep_t = jnp.exp(top_t - top)
        attended = (acc_f * keep_f + acc_t * keep_t) / (total_f * keep_f + total_t * keep_t)
        head_outputs.append(attended.astype(jnp.bfloat16))
    attended_all = jnp.concatenate(head_outputs, axis=1)
    ys = lax.axis_size("y")
    xs = lax.axis_size("x")
    w5 = weight_pair.reshape(2, width, xs, ys, block)
    partial_out = jnp.einsum("rk,ckxyn->yrcxn", attended_all, w5, preferred_element_type=jnp.float32)
    partial_out = partial_out.reshape(groups, rows, -1)
    mixed = lax.psum_scatter(partial_out.astype(jnp.bfloat16), "head", scatter_dimension=0, tiled=True)
    mixed = mixed.reshape(rows, 2, xs, block)
    mixed = jnp.where(first_core, mixed, mixed[:, ::-1])
    return mixed.transpose(0, 2, 1, 3).reshape(rows, -1)


def solution(mesh):
    frames, heads = mesh.devices.shape
    cores = 2
    xs = 4 if frames % (4 * cores) == 0 else 1
    grid = mesh.devices.reshape(frames // (xs * cores), xs, cores, heads)
    fine = jax.sharding.Mesh(grid, FRAME_AXES + ("head",))
    return jax.shard_map(
        on_device,
        mesh=fine,
        in_specs=(
            P(FRAME_AXES, "head"),
            P(FRAME_AXES, "head"),
            P(FRAME_AXES, "head"),
            P(FRAME_AXES, "head"),
            P(FRAME_AXES, "head"),
            P("head", FRAME_AXES),
            P(),
            P(),
        ),
        out_specs=P(FRAME_AXES, "head"),
        check_vma=False,
    )
```

```python
import math

import jax
import jax.numpy as jnp
from jax import lax
from jax.sharding import PartitionSpec as P

HD = 128
WIN = 4
FRAME_AXES = ("y", "x", "c")
CHIP_AXES = ("y", "x")
GATHER_SPARE = 8


def shift_frames(value, steps):
    count = lax.axis_size(FRAME_AXES)
    return lax.ppermute(value, FRAME_AXES, [(source, source + steps) for source in range(count - steps)])


def relay_back(value, chips_back):
    ys, xs, cs = (lax.axis_size(name) for name in FRAME_AXES)
    count = ys * xs * cs
    first, second = [], []
    for y in range(ys):
        for x in range(xs):
            for c in range(cs):
                source = (y * xs + x) * cs + c
                middle = (y * xs + (x - 1) % xs) * cs + c
                first.append((source, middle))
                target = source + chips_back * cs
                if target < count:
                    second.append((middle, target))
    hop = lax.ppermute(value, FRAME_AXES, first)
    return lax.ppermute(hop, FRAME_AXES, second)


def swap_cores(value):
    return lax.ppermute(value, "c", [(0, 1), (1, 0)])


def on_device(queries, keys, values, text_keys, text_values, out_weight, windows, lengths):
    rows = queries.shape[0]
    width = queries.shape[1]
    local_heads = width // HD
    groups = lax.axis_size("head")
    scale = 1.0 / math.sqrt(HD)
    position = lax.axis_index(FRAME_AXES)
    core = lax.axis_index("c")
    first_core = core == 0

    chips = lax.axis_size(CHIP_AXES)
    block = out_weight.shape[1]
    tokens = text_keys.shape[0]
    spare = jnp.zeros((width, GATHER_SPARE), out_weight.dtype)
    packed = jnp.concatenate([out_weight, text_keys.T, text_values.T, spare], axis=1)
    packed, keys, values = lax.optimization_barrier((packed, keys, values))
    packed = lax.all_gather(lax.all_gather(packed, "y", axis=1, tiled=True), "x", axis=1, tiled=True)
    own = jnp.stack([keys, values])
    back2 = shift_frames(own, 2)
    back4 = relay_back(own, 2)
    back1 = swap_cores(jnp.where(first_core, own, back2))
    back3 = swap_cores(jnp.where(first_core, back2, back4))
    kv_list = [own, back1, back2, back3, back4]

    token_ids = jnp.arange(rows, dtype=jnp.int32)
    own_window = windows[position]
    mask_list = []
    for step in range(WIN + 1):
        source = position - step
        usable = (step <= own_window) & (source >= 0)
        source_len = lengths[jnp.maximum(source, 0)]
        mask_list.append(usable & (token_ids < source_len))
    key_mask = jnp.concatenate(mask_list)
    all_keys = jnp.concatenate([p[0] for p in kv_list], axis=0)
    all_values = jnp.concatenate([p[1] for p in kv_list], axis=0)
    frame_parts = []
    for head_index in range(local_heads):
        lower = head_index * HD
        query_h = queries[:, lower : lower + HD]
        scores = lax.dot_general(
            query_h, all_keys[:, lower : lower + HD], (((1,), (1,)), ((), ())),
            preferred_element_type=jnp.float32) * scale
        scores = jnp.where(key_mask[None, :], scores, -jnp.inf)
        top_f = jnp.max(scores, axis=-1, keepdims=True)
        weights = jnp.exp(scores - top_f)
        total_f = jnp.sum(weights, axis=-1, keepdims=True)
        acc_f = jnp.dot(weights.astype(jnp.bfloat16), all_values[:, lower : lower + HD],
                        preferred_element_type=jnp.float32)
        frame_parts.append((top_f, total_f, acc_f))

    packed, frame_parts = lax.optimization_barrier((packed, frame_parts))
    packed = packed.reshape(width, chips, -1)
    text_own = packed[:, :, block : block + 2 * tokens]
    text_pair = jnp.stack([text_own, swap_cores(text_own)])
    text_kt = text_pair[:, :, :, :tokens].transpose(1, 0, 2, 3).reshape(width, -1)
    text_vt = text_pair[:, :, :, tokens:].transpose(1, 0, 2, 3).reshape(width, -1)
    weight_own = packed[:, :, :block]
    weight_other = swap_cores(weight_own)
    weight_pair = jnp.where(first_core, jnp.stack([weight_own, weight_other]), jnp.stack([weight_other, weight_own]))

    head_outputs = []
    for head_index in range(local_heads):
        lower = head_index * HD
        query_h = queries[:, lower : lower + HD]
        top_f, total_f, acc_f = frame_parts[head_index]
        scores_t = jnp.dot(query_h, text_kt[lower : lower + HD], preferred_element_type=jnp.float32) * scale
        top_t = jnp.max(scores_t, axis=-1, keepdims=True)
        weights_t = jnp.exp(scores_t - top_t)
        total_t = jnp.sum(weights_t, axis=-1, keepdims=True)
        acc_t = lax.dot_general(
            weights_t.astype(jnp.bfloat16), text_vt[lower : lower + HD], (((1,), (1,)), ((), ())),
            preferred_element_type=jnp.float32)
        top = jnp.maximum(top_f, top_t)
        keep_f = jnp.exp(top_f - top)
        keep_t = jnp.exp(top_t - top)
        attended = (acc_f * keep_f + acc_t * keep_t) / (total_f * keep_f + total_t * keep_t)
        head_outputs.append(attended.astype(jnp.bfloat16))
    attended_all = jnp.concatenate(head_outputs, axis=1)
    ys = lax.axis_size("y")
    xs = lax.axis_size("x")
    w5 = weight_pair.reshape(2, width, xs, ys, block)
    partial_out = jnp.einsum("rk,ckxyn->yrcxn", attended_all, w5, preferred_element_type=jnp.float32)
    partial_out = partial_out.reshape(groups, rows, -1)
    mixed = lax.psum_scatter(partial_out.astype(jnp.bfloat16), "head", scatter_dimension=0, tiled=True)
    mixed = mixed.reshape(rows, 2, xs, block)
    return mixed.transpose(0, 2, 1, 3).reshape(rows, -1)


def solution(mesh):
    frames, heads = mesh.devices.shape
    cores = 2
    xs = 4 if frames % (4 * cores) == 0 else 1
    grid = mesh.devices.reshape(frames // (xs * cores), xs, cores, heads)
    fine = jax.sharding.Mesh(grid, FRAME_AXES + ("head",))
    return jax.shard_map(
        on_device,
        mesh=fine,
        in_specs=(
            P(FRAME_AXES, "head"),
            P(FRAME_AXES, "head"),
            P(FRAME_AXES, "head"),
            P(FRAME_AXES, "head"),
            P(FRAME_AXES, "head"),
            P("head", FRAME_AXES),
            P(),
            P(),
        ),
        out_specs=P(FRAME_AXES, "head"),
        check_vma=False,
    )
```
